256 devices in a mesh: req: 32 (over x, z), tp: 8 (over y, core).
Axes of the slice: x: 4, y: 4, z: 8, core: 2. Of those that a mesh axis runs over, the one named last changes fastest.
Arguments:
- queries: bfloat16 [2048, 8192], P('req', 'tp'), may hold values from -5 to 5
- key_cache: bfloat16 [2048, 64, 1024], P('req', None, 'tp'), may hold values from -5 to 5
- value_cache: bfloat16 [2048, 64, 1024], P('req', None, 'tp'), may hold values from -5 to 5
- lengths: int32 [2048], P('req'), may hold values from 8 to 64, as said below
- row_adapter_index: int32 [2048], replicated, may hold values from 0 to 1023, as said below
- down_weight: bfloat16 [1024, 8192, 64], P('req', 'tp'), may hold values from -0.0625 to 0.0625
- up_weight: bfloat16 [1024, 64, 8192], P('req', None, 'tp'), may hold values from -1.5 to 1.5
Outputs:
- attn_out: bfloat16 [2048, 8192], P('req', 'tp')
- adapter_output: bfloat16 [2048, 8192], P('req', 'tp')
The draws below stay inside these ranges and needn't reach their ends.
Inputs may be any that keep to these rules, and one draw needn't show every extreme that they name: `row_adapter_index`: adapter a belongs to owner a // 32, the index of req that holds it. Among the 64 rows of one index of req (aligned blocks of the row dimension), at most 8 name adapters of one owner; some owner receives exactly 8 rows from every block. `lengths`: every index of req holds a row of length 64.
All inputs are finite; a program needn't handle non-finite values.
Results may differ from the reference program's by a relative error of at most 0.019.
Values may be sent and summed in bfloat16 or wider, within the bound.
No kernel may reach another device: no remote copies, remote signals or barrier semaphores. Data moves between devices by JAX's collectives and lax.ppermute only.
A program may use at most 64 MiB of HBM per device.

```python
import jax
import jax.numpy as jnp
from jax import lax

MODEL_WIDTH = 8192
HEADS = 64
KV_HEADS = 8
HEAD_DIM = 128
ADAPTER_RANK = 64
CAP = 8
ROWS_PER_INDEX = 64
CTX = 64
ADP_REQ = 32
GROUP = 8
REQUEST_ROWS = 2048
ADAPTER_TOTAL = 1024
N_REQ = 32


def query_key_parts(key):
    key_q, key_k = jax.random.split(key, 2)
    width_kv = KV_HEADS * HEAD_DIM
    queries = jnp.clip(jax.random.normal(key_q, (REQUEST_ROWS, HEADS * HEAD_DIM), jnp.float32), -5.0, 5.0)
    keys = jnp.clip(jax.random.normal(key_k, (REQUEST_ROWS, CTX, width_kv), jnp.float32), -5.0, 5.0)
    return (queries, keys)


def draw_queries(key, part):
    return query_key_parts(jax.random.fold_in(key, 11))[0].astype(jnp.bfloat16)


def draw_key_cache(key, part):
    return query_key_parts(jax.random.fold_in(key, 11))[1].astype(jnp.bfloat16)


def draw_lengths(key, part):
    key_a, key_b, key_c = jax.random.split(key, 3)
    first = jax.random.randint(key_a, (REQUEST_ROWS,), 0, CTX - 7)
    second = jax.random.randint(key_b, (REQUEST_ROWS,), 0, CTX - 7)
    lengths = 8 + first * second // (CTX - 8)
    longest = jax.random.randint(key_c, (N_REQ,), 0, ROWS_PER_INDEX)
    places = jnp.arange(N_REQ) * ROWS_PER_INDEX + longest
    return lengths.at[places].set(CTX).astype(jnp.int32)


def draw_row_adapter_index(key, part):
    key_h, key_n, key_t, key_p, key_f, key_a, key_b = jax.random.split(key, 7)
    slot_total = N_REQ * CAP
    heat = jax.random.randint(key_h, (N_REQ,), 0, 3)
    leader = jax.random.randint(key_t, (), 0, N_REQ)
    owner_of_slot = jnp.arange(slot_total) // CAP
    noise = jax.random.randint(key_n, (N_REQ, N_REQ), 0, 3)

    def one_block(noise_row, block_key):
        key_x, key_y = jax.random.split(block_key)
        level = heat[owner_of_slot] + noise_row[owner_of_slot] + 8 * (owner_of_slot == leader).astype(jnp.int32)
        score = level * slot_total + jax.random.permutation(key_x, slot_total)
        picked = lax.top_k(score, ROWS_PER_INDEX)[1]
        owners = picked // CAP
        return owners[jax.random.permutation(key_y, ROWS_PER_INDEX)]
    owners = jax.vmap(one_block)(noise, jax.random.split(key_p, N_REQ)).reshape(REQUEST_ROWS)
    favorite = jax.random.randint(key_f, (N_REQ,), 0, ADP_REQ)
    lower = jnp.minimum(jax.random.randint(key_a, (REQUEST_ROWS,), 0, ADP_REQ), jax.random.randint(key_b, (REQUEST_ROWS,), 0, ADP_REQ))
    local = (lower + favorite[owners]) % ADP_REQ
    return (owners * ADP_REQ + local).astype(jnp.int32)


def levels(own_key, shape, pieces, least, largest):
    gain = 1.0
    for position, blocks in pieces:
        heights = jax.random.uniform(jax.random.fold_in(jax.random.fold_in(own_key, 6), position), (blocks,), jnp.float32, least / len(pieces), largest / len(pieces))
        gain = gain * jnp.repeat(jnp.exp(heights), shape[position] // blocks).reshape((-1,) + (1,) * (len(shape) - 1 - position))
    return gain


def normal_values(key, shape, spread, bound, shards=(), kind=jnp.bfloat16):
    entries = spread * jax.random.normal(key, shape, jnp.float32)
    if shards:
        entries = entries * levels(key, shape, shards, -0.22, 0.18)
    return jnp.clip(entries, -bound, bound).astype(kind)


def setup_inputs(seed: int = 0) -> dict:
    arg_keys = jax.random.split(jax.random.key(seed), 8)
    queries = draw_queries(jax.random.fold_in(arg_keys[7], 71), 0)
    key_cache = draw_key_cache(jax.random.fold_in(arg_keys[7], 71), 0)
    value_cache = normal_values(arg_keys[2], (REQUEST_ROWS, CTX, KV_HEADS * HEAD_DIM), 1.0, 5.0, ((0, 32), (2, 8)))
    lengths = draw_lengths(jax.random.fold_in(arg_keys[7], 71), 0)
    row_adapter_index = draw_row_adapter_index(jax.random.fold_in(arg_keys[7], 71), 0)
    down_weight = normal_values(arg_keys[5], (ADAPTER_TOTAL, MODEL_WIDTH, ADAPTER_RANK), MODEL_WIDTH ** -0.5, 0.0625, ((0, 32), (1, 8)))
    up_weight = normal_values(arg_keys[6], (ADAPTER_TOTAL, ADAPTER_RANK, MODEL_WIDTH), (ADAPTER_RANK // 4) ** -0.5, 1.5, ((0, 32), (2, 8)))
    return {"queries": queries, "key_cache": key_cache, "value_cache": value_cache, "lengths": lengths, "row_adapter_index": row_adapter_index, "down_weight": down_weight, "up_weight": up_weight}


def attend_block(block):
    query_rows, key_rows, value_rows, length_rows = block
    count = query_rows.shape[0]
    query_heads = query_rows.reshape(count, KV_HEADS, GROUP, HEAD_DIM).astype(jnp.float32)
    key_heads = key_rows.reshape(count, CTX, KV_HEADS, HEAD_DIM).astype(jnp.float32)
    value_heads = value_rows.reshape(count, CTX, KV_HEADS, HEAD_DIM).astype(jnp.float32)
    scores = jnp.einsum("rkgd,rckd->rkgc", query_heads, key_heads) * (HEAD_DIM ** -0.5)
    valid = jnp.arange(CTX)[None, :] < length_rows[:, None]
    scores = jnp.where(valid[:, None, None, :], scores, -jnp.inf)
    highest = jnp.max(scores, axis=3, keepdims=True)
    expo = jnp.exp(scores - highest)
    weights = (expo / jnp.sum(expo, axis=3, keepdims=True)).astype(jnp.bfloat16)
    mixed = jnp.einsum("rkgc,rckd->rkgd", weights.astype(jnp.float32), value_heads)
    return mixed.astype(jnp.bfloat16).reshape(count, MODEL_WIDTH)


def reference(queries, key_cache, value_cache, lengths, row_adapter_index, down_weight, up_weight):
    block_list = REQUEST_ROWS // ROWS_PER_INDEX
    width_kv = KV_HEADS * HEAD_DIM
    decode_attention = lax.map(attend_block, (queries.reshape(block_list, ROWS_PER_INDEX, MODEL_WIDTH),
                                  key_cache.reshape(block_list, ROWS_PER_INDEX, CTX, width_kv),
                                  value_cache.reshape(block_list, ROWS_PER_INDEX, CTX, width_kv),
                                  lengths.reshape(block_list, ROWS_PER_INDEX)))
    decode_attention = decode_attention.reshape(REQUEST_ROWS, MODEL_WIDTH)

    def apply_adapter_block(block):
        rows_in, incoming_index = block
        down_matrices = down_weight[incoming_index.astype(jnp.int32)].astype(jnp.float32)
        shrink = jnp.einsum("bd,bdr->br", rows_in.astype(jnp.float32), down_matrices).astype(jnp.bfloat16)
        up_matrices = up_weight[incoming_index.astype(jnp.int32)].astype(jnp.float32)
        return jnp.einsum("br,bre->be", shrink.astype(jnp.float32), up_matrices).astype(jnp.bfloat16)

    low_rank_term = lax.map(apply_adapter_block, (decode_attention.reshape(block_list, ROWS_PER_INDEX, MODEL_WIDTH), row_adapter_index.reshape(block_list, ROWS_PER_INDEX)))
    return decode_attention, low_rank_term.reshape(REQUEST_ROWS, MODEL_WIDTH)
```

```python
import jax
import jax.numpy as jnp
from jax import lax
from jax.sharding import PartitionSpec as P

HEAD_DIM = 128
CAP = 8
ROWS_PER_INDEX = 64
CTX = 64
ADP_REQ = 32
GROUP = 8


def attend(queries, key_cache, value_cache, lengths):
    count = queries.shape[0]
    kv_local = key_cache.shape[2] // HEAD_DIM
    query_heads = queries.reshape(count, kv_local, GROUP, HEAD_DIM)
    key_heads = key_cache.reshape(count, CTX, kv_local, HEAD_DIM)
    value_heads = value_cache.reshape(count, CTX, kv_local, HEAD_DIM)
    scores = jnp.einsum(
        "rkgd,rckd->rkgc", query_heads, key_heads, preferred_element_type=jnp.float32
    ) * HEAD_DIM ** (-0.5)
    valid = jnp.arange(CTX)[None, :] < lengths[:, None]
    scores = jnp.where(valid[:, None, None, :], scores, -jnp.inf)
    highest = jnp.max(scores, axis=3, keepdims=True)
    expo = jnp.exp(scores - highest)
    weights = (expo / jnp.sum(expo, axis=3, keepdims=True)).astype(jnp.bfloat16)
    mixed = jnp.einsum("rkgc,rckd->rkgd", weights, value_heads, preferred_element_type=jnp.float32)
    return mixed.astype(jnp.bfloat16).reshape(count, kv_local * GROUP * HEAD_DIM)


def apply_adapter(incoming_slots, adapter_of_slot, down_weight, up_weight):
    adapter_grouped = jnp.einsum(
        "pv,hvo->pho", incoming_slots, down_weight, preferred_element_type=jnp.float32
    )
    partial_shrink = jnp.einsum("sar,sa->sr", adapter_grouped, adapter_of_slot)
    shrink = lax.psum(partial_shrink, "tp").astype(jnp.bfloat16)
    spread_rows = shrink[:, None, :] * adapter_of_slot.astype(jnp.bfloat16)[:, :, None]
    return jnp.einsum(
        "fmb,mbc->fc", spread_rows, up_weight, preferred_element_type=jnp.float32
    ).astype(jnp.bfloat16)


def slot_ranks(owners):
    order = jnp.arange(owners.shape[-1])
    earlier = order[None, :] < order[:, None]
    same_owner = owners[..., :, None] == owners[..., None, :]
    return jnp.sum(jnp.logical_and(same_owner, earlier), axis=-1)


def on_device(queries, key_cache, value_cache, lengths, row_adapter_index, down_weight, up_weight):
    decode_attention = attend(queries, key_cache, value_cache, lengths)
    n_req = lax.axis_size("req")
    my_index = lax.axis_index("req")
    slot_total = n_req * CAP
    block_list = row_adapter_index.reshape(n_req, ROWS_PER_INDEX)
    owners = block_list // ADP_REQ
    ranks = slot_ranks(owners)

    recv_slot = jnp.where(owners == my_index, jnp.arange(n_req)[:, None] * CAP + ranks, -1).reshape(
        n_req * ROWS_PER_INDEX
    )
    recv_onehot = (jnp.arange(slot_total)[:, None] == recv_slot[None, :]).astype(jnp.bfloat16)
    local_adapter = row_adapter_index % ADP_REQ
    adapter_onehot = (local_adapter[:, None] == jnp.arange(ADP_REQ)[None, :]).astype(jnp.bfloat16)
    adapter_of_slot = jnp.dot(recv_onehot, adapter_onehot, preferred_element_type=jnp.float32)

    my_owners = lax.dynamic_index_in_dim(owners, my_index, 0, keepdims=False)
    my_ranks = lax.dynamic_index_in_dim(ranks, my_index, 0, keepdims=False)
    send_slot = my_owners * CAP + my_ranks
    send_onehot = (jnp.arange(slot_total)[:, None] == send_slot[None, :]).astype(jnp.bfloat16)
    packed = jnp.dot(send_onehot, decode_attention, preferred_element_type=jnp.float32).astype(
        jnp.bfloat16
    )
    width = packed.shape[1]
    gathered_rows = lax.all_to_all(
        packed.reshape(n_req, CAP, width), "req", 0, 0, tiled=True
    ).reshape(slot_total, width)
    adapter_delta = apply_adapter(gathered_rows, adapter_of_slot, down_weight, up_weight)
    returned = lax.all_to_all(
        adapter_delta.reshape(n_req, CAP, width), "req", 0, 0, tiled=True
    ).reshape(slot_total, width)
    adapter_output = lax.dot_general(
        send_onehot, returned, (((0,), (0,)), ((), ())), preferred_element_type=jnp.float32
    ).astype(jnp.bfloat16)
    return (decode_attention, adapter_output)


def solution(mesh):
    in_specs = (
        P("req", "tp"),
        P("req", None, "tp"),
        P("req", None, "tp"),
        P("req"),
        P(),
        P("req", "tp", None),
        P("req", None, "tp"),
    )
    out_specs = (P("req", "tp"), P("req", "tp"))
    return jax.shard_map(
        on_device, mesh=mesh, in_specs=in_specs, out_specs=out_specs, check_vma=False
    )
```

```python
import jax
import jax.numpy as jnp
from jax import lax
from jax.sharding import PartitionSpec as P

HEAD_DIM = 128
CAP = 8
ROWS_PER_INDEX = 64
CTX = 64
ADP_REQ = 32
GROUP = 8


def attend(queries, key_cache, value_cache, lengths):
    count = queries.shape[0]
    kv_local = key_cache.shape[2] // HEAD_DIM
    query_heads = queries.reshape(count, kv_local, GROUP, HEAD_DIM)
    key_heads = key_cache.reshape(count, CTX, kv_local, HEAD_DIM)
    value_heads = value_cache.reshape(count, CTX, kv_local, HEAD_DIM)
    scores = jnp.einsum(
        "rkgd,rckd->rkgc", query_heads, key_heads, preferred_element_type=jnp.float32
    ) * HEAD_DIM ** (-0.5)
    valid = jnp.arange(CTX)[None, :] < lengths[:, None]
    scores = jnp.where(valid[:, None, None, :], scores, -jnp.inf)
    highest = jnp.max(scores, axis=3, keepdims=True)
    expo = jnp.exp(scores - highest)
    weights = (expo / jnp.sum(expo, axis=3, keepdims=True)).astype(jnp.bfloat16)
    mixed = jnp.einsum("rkgc,rckd->rkgd", weights, value_heads, preferred_element_type=jnp.float32)
    return mixed.astype(jnp.bfloat16).reshape(count, kv_local * GROUP * HEAD_DIM)


def tree_sum(value, axis):
    size = lax.axis_size(axis)
    step = 1
    while step < size:
        pairs = [(i, i ^ step) for i in range(size)]
        value = value + lax.ppermute(value, axis, pairs)
        step *= 2
    return value


def apply_adapter(incoming_slots, adapter_of_slot, down_weight, up_weight):
    adapter_grouped = jnp.einsum(
        "pv,hvo->pho", incoming_slots, down_weight, preferred_element_type=jnp.float32
    )
    partial_shrink = jnp.einsum("sar,sa->sr", adapter_grouped, adapter_of_slot)
    shrink = tree_sum(partial_shrink, "tp").astype(jnp.bfloat16)
    spread_rows = shrink[:, None, :] * adapter_of_slot.astype(jnp.bfloat16)[:, :, None]
    return jnp.einsum(
        "fmb,mbc->fc", spread_rows, up_weight, preferred_element_type=jnp.float32
    ).astype(jnp.bfloat16)


def slot_ranks(owners):
    order = jnp.arange(owners.shape[-1])
    earlier = order[None, :] < order[:, None]
    same_owner = owners[..., :, None] == owners[..., None, :]
    return jnp.sum(jnp.logical_and(same_owner, earlier), axis=-1)


def on_device(queries, key_cache, value_cache, lengths, row_adapter_index, down_weight, up_weight):
    decode_attention = attend(queries, key_cache, value_cache, lengths)
    n_req = lax.axis_size("req")
    my_index = lax.axis_index("req")
    slot_total = n_req * CAP
    block_list = row_adapter_index.reshape(n_req, ROWS_PER_INDEX)
    owners = block_list // ADP_REQ
    ranks = slot_ranks(owners)

    recv_slot = jnp.where(owners == my_index, jnp.arange(n_req)[:, None] * CAP + ranks, -1).reshape(
        n_req * ROWS_PER_INDEX
    )
    recv_onehot = (jnp.arange(slot_total)[:, None] == recv_slot[None, :]).astype(jnp.bfloat16)
    local_adapter = row_adapter_index % ADP_REQ
    adapter_onehot = (local_adapter[:, None] == jnp.arange(ADP_REQ)[None, :]).astype(jnp.bfloat16)
    adapter_of_slot = jnp.dot(recv_onehot, adapter_onehot, preferred_element_type=jnp.float32)

    my_owners = lax.dynamic_index_in_dim(owners, my_index, 0, keepdims=False)
    my_ranks = lax.dynamic_index_in_dim(ranks, my_index, 0, keepdims=False)
    send_slot = my_owners * CAP + my_ranks
    send_onehot = (jnp.arange(slot_total)[:, None] == send_slot[None, :]).astype(jnp.bfloat16)
    packed = jnp.dot(send_onehot, decode_attention, preferred_element_type=jnp.float32).astype(
        jnp.bfloat16
    )
    width = packed.shape[1]
    gathered_rows = lax.all_to_all(
        packed.reshape(n_req, CAP, width), "req", 0, 0, tiled=True
    ).reshape(slot_total, width)
    adapter_delta = apply_adapter(gathered_rows, adapter_of_slot, down_weight, up_weight)
    returned = lax.all_to_all(
        adapter_delta.reshape(n_req, CAP, width), "req", 0, 0, tiled=True
    ).reshape(slot_total, width)
    adapter_output = lax.dot_general(
        send_onehot, returned, (((0,), (0,)), ((), ())), preferred_element_type=jnp.float32
    ).astype(jnp.bfloat16)
    return (decode_attention, adapter_output)


def solution(mesh):
    in_specs = (
        P("req", "tp"),
        P("req", None, "tp"),
        P("req", None, "tp"),
        P("req"),
        P(),
        P("req", "tp", None),
        P("req", None, "tp"),
    )
    out_specs = (P("req", "tp"), P("req", "tp"))
    return jax.shard_map(
        on_device, mesh=mesh, in_specs=in_specs, out_specs=out_specs, check_vma=False
    )
```

```python
import jax
import jax.numpy as jnp
from jax import lax
from jax.sharding import PartitionSpec as P


HEAD_DIM = 128
CAP = 8
ROWS_PER_INDEX = 64
CTX = 64
ADP_REQ = 32
GROUP = 8


def attend(queries, key_cache, value_cache, lengths):
    count = queries.shape[0]
    kv_local = key_cache.shape[2] // HEAD_DIM
    query_heads = queries.reshape(count, kv_local, GROUP, HEAD_DIM)
    key_heads = key_cache.reshape(count, CTX, kv_local, HEAD_DIM)
    value_heads = value_cache.reshape(count, CTX, kv_local, HEAD_DIM)
    scores = jnp.einsum(
        "rkgd,rckd->rkgc", query_heads, key_heads, preferred_element_type=jnp.float32
    ) * HEAD_DIM ** (-0.5)
    valid = jnp.arange(CTX)[None, :] < lengths[:, None]
    scores = jnp.where(valid[:, None, None, :], scores, -jnp.inf)
    highest = jnp.max(scores, axis=3, keepdims=True)
    expo = jnp.exp(scores - highest)
    weights = (expo / jnp.sum(expo, axis=3, keepdims=True)).astype(jnp.bfloat16)
    mixed = jnp.einsum("rkgc,rckd->rkgd", weights, value_heads, preferred_element_type=jnp.float32)
    return mixed.astype(jnp.bfloat16).reshape(count, kv_local * GROUP * HEAD_DIM)


def direct_sum(value, axis):
    size = lax.axis_size(axis)
    me = lax.axis_index(axis)
    parts = [value] + [
        lax.ppermute(value, axis, [(i, (i - shift) % size) for i in range(size)])
        for shift in range(1, size)
    ]
    stacked = jnp.stack(parts, axis=0)
    stacked = jnp.roll(stacked, me, axis=0)
    return jnp.sum(stacked, axis=0)


def apply_adapter(incoming_slots, adapter_of_slot, down_weight, up_weight):
    adapter_grouped = jnp.einsum(
        "pv,hvo->pho", incoming_slots, down_weight, preferred_element_type=jnp.float32
    )
    partial_shrink = jnp.einsum("sar,sa->sr", adapter_grouped, adapter_of_slot)
    shrink = direct_sum(partial_shrink, "tp").astype(jnp.bfloat16)
    spread_rows = shrink[:, None, :] * adapter_of_slot.astype(jnp.bfloat16)[:, :, None]
    return jnp.einsum(
        "fmb,mbc->fc", spread_rows, up_weight, preferred_element_type=jnp.float32
    ).astype(jnp.bfloat16)


def slot_ranks(owners):
    order = jnp.arange(owners.shape[-1])
    earlier = order[None, :] < order[:, None]
    same_owner = owners[..., :, None] == owners[..., None, :]
    return jnp.sum(jnp.logical_and(same_owner, earlier), axis=-1)


def on_device(queries, key_cache, value_cache, lengths, row_adapter_index, down_weight, up_weight):
    decode_attention = attend(queries, key_cache, value_cache, lengths)
    n_req = lax.axis_size("req")
    my_index = lax.axis_index("req")
    slot_total = n_req * CAP
    block_list = row_adapter_index.reshape(n_req, ROWS_PER_INDEX)
    owners = block_list // ADP_REQ
    ranks = slot_ranks(owners)

    recv_slot = jnp.where(owners == my_index, jnp.arange(n_req)[:, None] * CAP + ranks, -1).reshape(
        n_req * ROWS_PER_INDEX
    )
    recv_onehot = (jnp.arange(slot_total)[:, None] == recv_slot[None, :]).astype(jnp.bfloat16)
    local_adapter = row_adapter_index % ADP_REQ
    adapter_onehot = (local_adapter[:, None] == jnp.arange(ADP_REQ)[None, :]).astype(jnp.bfloat16)
    adapter_of_slot = jnp.dot(recv_onehot, adapter_onehot, preferred_element_type=jnp.float32)

    my_owners = lax.dynamic_index_in_dim(owners, my_index, 0, keepdims=False)
    my_ranks = lax.dynamic_index_in_dim(ranks, my_index, 0, keepdims=False)
    send_slot = my_owners * CAP + my_ranks
    send_onehot = (jnp.arange(slot_total)[:, None] == send_slot[None, :]).astype(jnp.bfloat16)
    packed = jnp.dot(send_onehot, decode_attention, preferred_element_type=jnp.float32).astype(
        jnp.bfloat16
    )
    width = packed.shape[1]
    gathered_rows = lax.all_to_all(
        packed.reshape(n_req, CAP, width), "req", 0, 0, tiled=True
    ).reshape(slot_total, width)
    adapter_delta = apply_adapter(gathered_rows, adapter_of_slot, down_weight, up_weight)
    returned = lax.all_to_all(
        adapter_delta.reshape(n_req, CAP, width), "req", 0, 0, tiled=True
    ).reshape(slot_total, width)
    adapter_output = lax.dot_general(
        send_onehot, returned, (((0,), (0,)), ((), ())), preferred_element_type=jnp.float32
    ).astype(jnp.bfloat16)
    return (decode_attention, adapter_output)


def solution(mesh):
    in_specs = (
        P("req", "tp"),
        P("req", None, "tp"),
        P("req", None, "tp"),
        P("req"),
        P(),
        P("req", "tp", None),
        P("req", None, "tp"),
    )
    out_specs = (P("req", "tp"), P("req", "tp"))
    return jax.shard_map(
        on_device, mesh=mesh, in_specs=in_specs, out_specs=out_specs, check_vma=False
    )
```

```python
import jax
import jax.numpy as jnp
from jax import lax
from jax.sharding import PartitionSpec as P

HEAD_DIM = 128
CAP = 8
ROWS_PER_INDEX = 64
CTX = 64
ADP_REQ = 32
GROUP = 8


def attend(queries, key_cache, value_cache, lengths):
    count = queries.shape[0]
    kv_local = key_cache.shape[2] // HEAD_DIM
    query_heads = queries.reshape(count, kv_local, GROUP, HEAD_DIM)
    key_heads = key_cache.reshape(count, CTX, kv_local, HEAD_DIM)
    value_heads = value_cache.reshape(count, CTX, kv_local, HEAD_DIM)
    scores = jnp.einsum(
        "rkgd,rckd->rkgc", query_heads, key_heads, preferred_element_type=jnp.float32
    ) * HEAD_DIM ** (-0.5)
    valid = jnp.arange(CTX)[None, :] < lengths[:, None]
    scores = jnp.where(valid[:, None, None, :], scores, -jnp.inf)
    highest = jnp.max(scores, axis=3, keepdims=True)
    expo = jnp.exp(scores - highest)
    weights = (expo / jnp.sum(expo, axis=3, keepdims=True)).astype(jnp.bfloat16)
    mixed = jnp.einsum("rkgc,rckd->rkgd", weights, value_heads, preferred_element_type=jnp.float32)
    return mixed.astype(jnp.bfloat16).reshape(count, kv_local * GROUP * HEAD_DIM)


def tree_sum(value, axis):
    size = lax.axis_size(axis)
    step = 1
    while step < size:
        pairs = [(i, i ^ step) for i in range(size)]
        value = value + lax.ppermute(value, axis, pairs)
        step *= 2
    return value


def apply_adapter(incoming_slots, adapter_of_slot, down_weight, up_weight):
    adapter_grouped = jnp.einsum(
        "pv,hvo->pho", incoming_slots, down_weight, preferred_element_type=jnp.float32
    )
    partial_shrink = jnp.einsum("sar,sa->sr", adapter_grouped, adapter_of_slot)
    shrink = tree_sum(partial_shrink, "tp").astype(jnp.bfloat16)
    spread_rows = shrink[:, None, :] * adapter_of_slot.astype(jnp.bfloat16)[:, :, None]
    return jnp.einsum(
        "fmb,mbc->fc", spread_rows, up_weight, preferred_element_type=jnp.float32
    ).astype(jnp.bfloat16)


def slot_ranks(owners):
    order = jnp.arange(owners.shape[-1])
    earlier = order[None, :] < order[:, None]
    same_owner = owners[..., :, None] == owners[..., None, :]
    return jnp.sum(jnp.logical_and(same_owner, earlier), axis=-1)


def on_device(queries, key_cache, value_cache, lengths, row_adapter_index, down_weight, up_weight):
    decode_attention = attend(queries, key_cache, value_cache, lengths)
    n_req = lax.axis_size("req")
    my_index = lax.axis_index("req")
    slot_total = n_req * CAP
    block_list = row_adapter_index.reshape(n_req, ROWS_PER_INDEX)
    owners = block_list // ADP_REQ
    ranks = slot_ranks(owners)

    recv_slot = jnp.where(owners == my_index, jnp.arange(n_req)[:, None] * CAP + ranks, -1).reshape(
        n_req * ROWS_PER_INDEX
    )
    recv_onehot = (jnp.arange(slot_total)[:, None] == recv_slot[None, :]).astype(jnp.bfloat16)
    local_adapter = row_adapter_index % ADP_REQ
    adapter_onehot = (local_adapter[:, None] == jnp.arange(ADP_REQ)[None, :]).astype(jnp.bfloat16)
    adapter_of_slot = jnp.dot(recv_onehot, adapter_onehot, preferred_element_type=jnp.float32)

    my_owners = lax.dynamic_index_in_dim(owners, my_index, 0, keepdims=False)
    my_ranks = lax.dynamic_index_in_dim(ranks, my_index, 0, keepdims=False)
    send_slot = my_owners * CAP + my_ranks
    send_onehot = (jnp.arange(slot_total)[:, None] == send_slot[None, :]).astype(jnp.bfloat16)
    packed = jnp.dot(send_onehot, decode_attention, preferred_element_type=jnp.float32).astype(
        jnp.bfloat16
    )
    packed, adapter_of_slot = lax.optimization_barrier((packed, adapter_of_slot))
    width = packed.shape[1]
    gathered_rows = lax.all_to_all(
        packed.reshape(n_req, CAP, width), "req", 0, 0, tiled=True
    ).reshape(slot_total, width)
    adapter_delta = apply_adapter(gathered_rows, adapter_of_slot, down_weight, up_weight)
    returned = lax.all_to_all(
        adapter_delta.reshape(n_req, CAP, width), "req", 0, 0, tiled=True
    ).reshape(slot_total, width)
    adapter_output = lax.dot_general(
        send_onehot, returned, (((0,), (0,)), ((), ())), preferred_element_type=jnp.float32
    ).astype(jnp.bfloat16)
    return (decode_attention, adapter_output)


def solution(mesh):
    in_specs = (
        P("req", "tp"),
        P("req", None, "tp"),
        P("req", None, "tp"),
        P("req"),
        P(),
        P("req", "tp", None),
        P("req", None, "tp"),
    )
    out_specs = (P("req", "tp"), P("req", "tp"))
    return jax.shard_map(
        on_device, mesh=mesh, in_specs=in_specs, out_specs=out_specs, check_vma=False
    )
```

```python
import jax
import jax.numpy as jnp
from jax import lax
from jax.sharding import PartitionSpec as P

HEAD_DIM = 128
CAP = 8
ROWS_PER_INDEX = 64
CTX = 64
ADP_REQ = 32
GROUP = 8


def attend(queries, key_cache, value_cache, lengths):
    count = queries.shape[0]
    kv_local = key_cache.shape[2] // HEAD_DIM
    query_heads = queries.reshape(count, kv_local, GROUP, HEAD_DIM)
    key_heads = key_cache.reshape(count, CTX, kv_local, HEAD_DIM)
    value_heads = value_cache.reshape(count, CTX, kv_local, HEAD_DIM)
    scores = jnp.einsum(
        "rkgd,rckd->rkgc", query_heads, key_heads, preferred_element_type=jnp.float32
    ) * HEAD_DIM ** (-0.5)
    valid = jnp.arange(CTX)[None, :] < lengths[:, None]
    scores = jnp.where(valid[:, None, None, :], scores, -jnp.inf)
    highest = jnp.max(scores, axis=3, keepdims=True)
    expo = jnp.exp(scores - highest)
    weights = (expo / jnp.sum(expo, axis=3, keepdims=True)).astype(jnp.bfloat16)
    mixed = jnp.einsum("rkgc,rckd->rkgd", weights, value_heads, preferred_element_type=jnp.float32)
    return mixed.astype(jnp.bfloat16).reshape(count, kv_local * GROUP * HEAD_DIM)


def tree_sum(value, axis):
    size = lax.axis_size(axis)
    step = 1
    while step < size:
        pairs = [(i, i ^ step) for i in range(size)]
        value = value + lax.ppermute(value, axis, pairs)
        step *= 2
    return value


def apply_adapter(incoming_slots, adapter_of_slot, down_weight, up_weight):
    adapter_grouped = jnp.einsum(
        "pv,hvo->pho", incoming_slots, down_weight, preferred_element_type=jnp.float32
    )
    partial_shrink = jnp.einsum("sar,sa->sr", adapter_grouped, adapter_of_slot)
    shrink = tree_sum(partial_shrink, "tp").astype(jnp.bfloat16)
    spread_rows = shrink[:, None, :] * adapter_of_slot.astype(jnp.bfloat16)[:, :, None]
    return jnp.einsum(
        "fmb,mbc->fc", spread_rows, up_weight, preferred_element_type=jnp.float32
    ).astype(jnp.bfloat16)


def on_device(queries, key_cache, value_cache, lengths, row_adapter_index, down_weight, up_weight):
    decode_attention = attend(queries, key_cache, value_cache, lengths)
    n_req = lax.axis_size("req")
    my_index = lax.axis_index("req")
    slot_total = n_req * CAP
    rows = ROWS_PER_INDEX
    owner_flat = lax.shift_right_logical(row_adapter_index, 5)
    local_flat = lax.bitwise_and(row_adapter_index, ADP_REQ - 1)
    owner_onehot = (owner_flat[:, None] == jnp.arange(n_req)[None, :]).astype(jnp.bfloat16)
    owner_onehot = owner_onehot.reshape(n_req, rows, n_req)
    local_onehot = (local_flat[:, None] == jnp.arange(ADP_REQ)[None, :]).astype(jnp.bfloat16)
    local_onehot = local_onehot.reshape(n_req, rows, ADP_REQ)
    order = jnp.arange(rows)
    earlier = (order[None, :] < order[:, None]).astype(jnp.bfloat16)
    counts = jnp.einsum("ij,bjo->bio", earlier, owner_onehot, preferred_element_type=jnp.float32)
    ranks = jnp.sum(counts * owner_onehot.astype(jnp.float32), axis=2)

    mine = lax.dynamic_index_in_dim(owner_onehot, my_index, 2, keepdims=False)
    pick = (ranks[:, None, :] == jnp.arange(CAP, dtype=jnp.float32)[None, :, None]).astype(jnp.bfloat16)
    pick = pick * mine[:, None, :]
    adapter_of_slot = jnp.einsum(
        "bki,bia->bka", pick, local_onehot, preferred_element_type=jnp.float32
    ).reshape(slot_total, ADP_REQ)

    my_owners = lax.dynamic_index_in_dim(owner_flat.reshape(n_req, rows), my_index, 0, keepdims=False)
    my_ranks = lax.dynamic_index_in_dim(ranks, my_index, 0, keepdims=False).astype(jnp.int32)
    send_slot = my_owners * CAP + my_ranks
    send_onehot = (jnp.arange(slot_total)[:, None] == send_slot[None, :]).astype(jnp.bfloat16)
    packed = jnp.dot(send_onehot, decode_attention, preferred_element_type=jnp.float32).astype(
        jnp.bfloat16
    )
    width = packed.shape[1]
    gathered_rows = lax.all_to_all(
        packed.reshape(n_req, CAP, width), "req", 0, 0, tiled=True
    ).reshape(slot_total, width)
    adapter_delta = apply_adapter(gathered_rows, adapter_of_slot, down_weight, up_weight)
    returned = lax.all_to_all(
        adapter_delta.reshape(n_req, CAP, width), "req", 0, 0, tiled=True
    ).reshape(slot_total, width)
    adapter_output = lax.dot_general(
        send_onehot, returned, (((0,), (0,)), ((), ())), preferred_element_type=jnp.float32
    ).astype(jnp.bfloat16)
    return (decode_attention, adapter_output)


def solution(mesh):
    in_specs = (
        P("req", "tp"),
        P("req", None, "tp"),
        P("req", None, "tp"),
        P("req"),
        P(),
        P("req", "tp", None),
        P("req", None, "tp"),
    )
    out_specs = (P("req", "tp"), P("req", "tp"))
    return jax.shard_map(
        on_device, mesh=mesh, in_specs=in_specs, out_specs=out_specs, check_vma=False
    )
```

```python
import jax
import jax.numpy as jnp
from jax import lax
from jax.experimental import pallas as pl
from jax.experimental.pallas import tpu as pltpu
from jax.sharding import PartitionSpec as P

HEAD_DIM = 128
CAP = 8
ROWS_PER_INDEX = 64
CTX = 64
ADP_REQ = 32
GROUP = 8


def attend(queries, key_cache, value_cache, lengths):
    count = queries.shape[0]
    kv_local = key_cache.shape[2] // HEAD_DIM
    query_heads = queries.reshape(count, kv_local, GROUP, HEAD_DIM)
    key_heads = key_cache.reshape(count, CTX, kv_local, HEAD_DIM)
    value_heads = value_cache.reshape(count, CTX, kv_local, HEAD_DIM)
    scores = jnp.einsum(
        "rkgd,rckd->rkgc", query_heads, key_heads, preferred_element_type=jnp.float32
    ) * HEAD_DIM ** (-0.5)
    valid = jnp.arange(CTX)[None, :] < lengths[:, None]
    scores = jnp.where(valid[:, None, None, :], scores, -jnp.inf)
    highest = jnp.max(scores, axis=3, keepdims=True)
    expo = jnp.exp(scores - highest)
    weights = (expo / jnp.sum(expo, axis=3, keepdims=True)).astype(jnp.bfloat16)
    mixed = jnp.einsum("rkgc,rckd->rkgd", weights, value_heads, preferred_element_type=jnp.float32)
    return mixed.astype(jnp.bfloat16).reshape(count, kv_local * GROUP * HEAD_DIM)


def tree_sum(value, axis):
    size = lax.axis_size(axis)
    step = 1
    while step < size:
        pairs = [(i, i ^ step) for i in range(size)]
        value = value + lax.ppermute(value, axis, pairs)
        step *= 2
    return value


def _down_body(x_ref, w_ref, sel_ref, o_ref):
    x = x_ref[...]
    acc = jnp.zeros(o_ref.shape, jnp.float32)
    for a in range(w_ref.shape[0]):
        part = lax.dot_general(
            x, w_ref[a], (((1,), (1,)), ((), ())), preferred_element_type=jnp.float32
        )
        acc = acc + part * sel_ref[:, a:a + 1]
    o_ref[...] = acc

def down_project(x, w, sel):
    slots, width = x.shape
    adapters, rank, _ = w.shape
    return pl.pallas_call(
        _down_body,
        out_shape=jax.ShapeDtypeStruct((slots, rank), jnp.float32),
        in_specs=[pl.BlockSpec(memory_space=pltpu.VMEM)] * 3,
        out_specs=pl.BlockSpec(memory_space=pltpu.VMEM),
        compiler_params=pltpu.CompilerParams(vmem_limit_bytes=48 * 1024 * 1024),
        cost_estimate=pl.CostEstimate(flops=2 * slots * width * rank * adapters, transcendentals=0,
                                      bytes_accessed=2 * (slots * width + adapters * width * rank) + 4 * slots * (adapters + rank)),
    )(x, w, sel)

def _up_body(s_ref, sel_ref, u_ref, o_ref):
    s = s_ref[...]
    acc = jnp.zeros(o_ref.shape, jnp.float32)
    for a in range(u_ref.shape[0]):
        acc = acc + jnp.dot(s * sel_ref[:, a:a + 1], u_ref[a], preferred_element_type=jnp.float32)
    o_ref[...] = acc.astype(o_ref.dtype)

def up_project(shrink, sel, u):
    slots, rank = shrink.shape
    adapters, _, width = u.shape
    return pl.pallas_call(
        _up_body,
        out_shape=jax.ShapeDtypeStruct((slots, width), jnp.bfloat16),
        in_specs=[pl.BlockSpec(memory_space=pltpu.VMEM)] * 3,
        out_specs=pl.BlockSpec(memory_space=pltpu.VMEM),
        compiler_params=pltpu.CompilerParams(vmem_limit_bytes=48 * 1024 * 1024),
        cost_estimate=pl.CostEstimate(flops=2 * slots * width * rank * adapters, transcendentals=0,
                                      bytes_accessed=2 * (slots * width + adapters * width * rank + slots * (adapters + rank))),
    )(shrink, sel, u)


def apply_adapter(incoming_slots, adapter_of_slot, down_weight, up_weight):
    partial_shrink = down_project(incoming_slots, jnp.swapaxes(down_weight, 1, 2), adapter_of_slot)
    shrink = tree_sum(partial_shrink, "tp").astype(jnp.bfloat16)
    return up_project(shrink, adapter_of_slot.astype(jnp.bfloat16), up_weight)


def on_device(queries, key_cache, value_cache, lengths, row_adapter_index, down_weight, up_weight):
    decode_attention = attend(queries, key_cache, value_cache, lengths)
    n_req = lax.axis_size("req")
    my_index = lax.axis_index("req")
    slot_total = n_req * CAP
    rows = ROWS_PER_INDEX
    owner_flat = lax.shift_right_logical(row_adapter_index, 5)
    local_flat = lax.bitwise_and(row_adapter_index, ADP_REQ - 1)
    owner_onehot = (owner_flat[:, None] == jnp.arange(n_req)[None, :]).astype(jnp.bfloat16)
    owner_onehot = owner_onehot.reshape(n_req, rows, n_req)
    local_onehot = (local_flat[:, None] == jnp.arange(ADP_REQ)[None, :]).astype(jnp.bfloat16)
    local_onehot = local_onehot.reshape(n_req, rows, ADP_REQ)
    order = jnp.arange(rows)
    earlier = (order[None, :] < order[:, None]).astype(jnp.bfloat16)
    counts = jnp.einsum("ij,bjo->bio", earlier, owner_onehot, preferred_element_type=jnp.float32)
    ranks = jnp.sum(counts * owner_onehot.astype(jnp.float32), axis=2)

    mine = lax.dynamic_index_in_dim(owner_onehot, my_index, 2, keepdims=False)
    pick = (ranks[:, None, :] == jnp.arange(CAP, dtype=jnp.float32)[None, :, None]).astype(jnp.bfloat16)
    pick = pick * mine[:, None, :]
    adapter_of_slot = jnp.einsum(
        "bki,bia->bka", pick, local_onehot, preferred_element_type=jnp.float32
    ).reshape(slot_total, ADP_REQ)

    my_owners = lax.dynamic_index_in_dim(owner_flat.reshape(n_req, rows), my_index, 0, keepdims=False)
    my_ranks = lax.dynamic_index_in_dim(ranks, my_index, 0, keepdims=False).astype(jnp.int32)
    send_slot = my_owners * CAP + my_ranks
    send_onehot = (jnp.arange(slot_total)[:, None] == send_slot[None, :]).astype(jnp.bfloat16)
    packed = jnp.dot(send_onehot, decode_attention, preferred_element_type=jnp.float32).astype(
        jnp.bfloat16
    )
    width = packed.shape[1]
    gathered_rows = lax.all_to_all(
        packed.reshape(n_req, CAP, width), "req", 0, 0, tiled=True
    ).reshape(slot_total, width)
    adapter_delta = apply_adapter(gathered_rows, adapter_of_slot, down_weight, up_weight)
    returned = lax.all_to_all(
        adapter_delta.reshape(n_req, CAP, width), "req", 0, 0, tiled=True
    ).reshape(slot_total, width)
    adapter_output = lax.dot_general(
        send_onehot, returned, (((0,), (0,)), ((), ())), preferred_element_type=jnp.float32
    ).astype(jnp.bfloat16)
    return (decode_attention, adapter_output)


def solution(mesh):
    in_specs = (
        P("req", "tp"),
        P("req", None, "tp"),
        P("req", None, "tp"),
        P("req"),
        P(),
        P("req", "tp", None),
        P("req", None, "tp"),
    )
    out_specs = (P("req", "tp"), P("req", "tp"))
    return jax.shard_map(
        on_device, mesh=mesh, in_specs=in_specs, out_specs=out_specs, check_vma=False
    )
```

```python
import jax
import jax.numpy as jnp
from jax import lax
from jax.sharding import PartitionSpec as P

HEAD_DIM = 128
CAP = 8
ROWS_PER_INDEX = 64
CTX = 64
ADP_REQ = 32
GROUP = 8


def attend(queries, key_cache, value_cache, lengths):
    count = queries.shape[0]
    kv_local = key_cache.shape[2] // HEAD_DIM
    query_heads = queries.reshape(count, kv_local, GROUP, HEAD_DIM)
    key_heads = key_cache.reshape(count, CTX, kv_local, HEAD_DIM)
    value_heads = value_cache.reshape(count, CTX, kv_local, HEAD_DIM)
    scores = jnp.einsum(
        "rkgd,rckd->rkgc", query_heads, key_heads, preferred_element_type=jnp.float32
    ) * HEAD_DIM ** (-0.5)
    valid = jnp.arange(CTX)[None, :] < lengths[:, None]
    scores = jnp.where(valid[:, None, None, :], scores, -jnp.inf)
    highest = jnp.max(scores, axis=3, keepdims=True)
    expo = jnp.exp(scores - highest)
    weights = (expo / jnp.sum(expo, axis=3, keepdims=True)).astype(jnp.bfloat16)
    mixed = jnp.einsum("rkgc,rckd->rkgd", weights, value_heads, preferred_element_type=jnp.float32)
    return mixed.astype(jnp.bfloat16).reshape(count, kv_local * GROUP * HEAD_DIM)


def tree_sum(value, axis):
    size = lax.axis_size(axis)
    step = 1
    while step < size:
        pairs = [(i, i ^ step) for i in range(size)]
        value = value + lax.ppermute(value, axis, pairs)
        step *= 2
    return value


def apply_adapter(incoming_slots, adapter_of_slot, down_weight, up_weight):
    adapter_grouped = jnp.einsum(
        "pv,hvo->pho", incoming_slots, down_weight, preferred_element_type=jnp.float32
    )
    partial_shrink = jnp.einsum("sar,sa->sr", adapter_grouped, adapter_of_slot)
    shrink = tree_sum(partial_shrink, "tp").astype(jnp.bfloat16)
    spread_rows = shrink[:, None, :] * adapter_of_slot.astype(jnp.bfloat16)[:, :, None]
    return jnp.einsum(
        "fmb,mbc->fc", spread_rows, up_weight, preferred_element_type=jnp.float32
    ).astype(jnp.bfloat16)


def slot_ranks(owners):
    order = jnp.arange(owners.shape[-1])
    earlier = order[None, :] < order[:, None]
    same_owner = owners[..., :, None] == owners[..., None, :]
    return jnp.sum(jnp.logical_and(same_owner, earlier), axis=-1)


def on_device(queries, key_cache, value_cache, lengths, row_adapter_index, down_weight, up_weight):
    decode_attention = attend(queries, key_cache, value_cache, lengths)
    n_req = lax.axis_size("req")
    my_index = lax.axis_index("req")
    slot_total = n_req * CAP
    block_list = row_adapter_index.reshape(n_req, ROWS_PER_INDEX)
    owners = lax.shift_right_logical(block_list, 5)
    ranks = slot_ranks(owners)

    recv_slot = jnp.where(owners == my_index, jnp.arange(n_req)[:, None] * CAP + ranks, -1).reshape(
        n_req * ROWS_PER_INDEX
    )
    recv_onehot = (jnp.arange(slot_total)[:, None] == recv_slot[None, :]).astype(jnp.bfloat16)
    local_adapter = lax.bitwise_and(row_adapter_index, ADP_REQ - 1)
    adapter_onehot = (local_adapter[:, None] == jnp.arange(ADP_REQ)[None, :]).astype(jnp.bfloat16)
    adapter_of_slot = jnp.dot(recv_onehot, adapter_onehot, preferred_element_type=jnp.float32)

    my_owners = lax.dynamic_index_in_dim(owners, my_index, 0, keepdims=False)
    my_ranks = lax.dynamic_index_in_dim(ranks, my_index, 0, keepdims=False)
    send_slot = my_owners * CAP + my_ranks
    send_onehot = (jnp.arange(slot_total)[:, None] == send_slot[None, :]).astype(jnp.bfloat16)
    packed = jnp.dot(send_onehot, decode_attention, preferred_element_type=jnp.float32).astype(
        jnp.bfloat16
    )
    width = packed.shape[1]
    gathered_rows = lax.all_to_all(
        packed.reshape(n_req, CAP, width), "req", 0, 0, tiled=True
    ).reshape(slot_total, width)
    adapter_delta = apply_adapter(gathered_rows, adapter_of_slot, down_weight, up_weight)
    returned = lax.all_to_all(
        adapter_delta.reshape(n_req, CAP, width), "req", 0, 0, tiled=True
    ).reshape(slot_total, width)
    adapter_output = lax.dot_general(
        send_onehot, returned, (((0,), (0,)), ((), ())), preferred_element_type=jnp.float32
    ).astype(jnp.bfloat16)
    return (decode_attention, adapter_output)


def solution(mesh):
    in_specs = (
        P("req", "tp"),
        P("req", None, "tp"),
        P("req", None, "tp"),
        P("req"),
        P(),
        P("req", "tp", None),
        P("req", None, "tp"),
    )
    out_specs = (P("req", "tp"), P("req", "tp"))
    return jax.shard_map(
        on_device, mesh=mesh, in_specs=in_specs, out_specs=out_specs, check_vma=False
    )
```

```python
import jax
import jax.numpy as jnp
from jax import lax
from jax.sharding import PartitionSpec as P

HEAD_DIM = 128
CAP = 8
ROWS_PER_INDEX = 64
CTX = 64
ADP_REQ = 32
GROUP = 8


def attend(queries, key_cache, value_cache, lengths):
    count = queries.shape[0]
    kv_local = key_cache.shape[2] // HEAD_DIM
    query_heads = queries.reshape(count, kv_local, GROUP, HEAD_DIM)
    key_heads = key_cache.reshape(count, CTX, kv_local, HEAD_DIM)
    value_heads = value_cache.reshape(count, CTX, kv_local, HEAD_DIM)
    scores = jnp.einsum(
        "rkgd,rckd->rkgc", query_heads, key_heads, preferred_element_type=jnp.float32
    ) * HEAD_DIM ** (-0.5)
    valid = jnp.arange(CTX)[None, :] < lengths[:, None]
    scores = jnp.where(valid[:, None, None, :], scores, -jnp.inf)
    highest = jnp.max(scores, axis=3, keepdims=True)
    expo = jnp.exp(scores - highest)
    weights = (expo / jnp.sum(expo, axis=3, keepdims=True)).astype(jnp.bfloat16)
    mixed = jnp.einsum("rkgc,rckd->rkgd", weights, value_heads, preferred_element_type=jnp.float32)
    return mixed.astype(jnp.bfloat16).reshape(count, kv_local * GROUP * HEAD_DIM)


def tree_sum(value, axis):
    size = lax.axis_size(axis)
    step = 1
    while step < size:
        pairs = [(i, i ^ step) for i in range(size)]
        value = value + lax.ppermute(value, axis, pairs)
        step *= 2
    return value


def apply_adapter(incoming_slots, adapter_of_slot, down_weight, up_weight):
    adapter_grouped = jnp.einsum(
        "pv,hvo->pho", incoming_slots, down_weight, preferred_element_type=jnp.float32
    )
    partial_shrink = jnp.einsum("sar,sa->sr", adapter_grouped, adapter_of_slot)
    shrink = tree_sum(partial_shrink, "tp").astype(jnp.bfloat16)
    spread_rows = shrink[:, None, :] * adapter_of_slot.astype(jnp.bfloat16)[:, :, None]
    return jnp.einsum(
        "fmb,mbc->fc", spread_rows, up_weight, preferred_element_type=jnp.float32
    ).astype(jnp.bfloat16)


def slot_ranks(owners):
    order = jnp.arange(owners.shape[-1])
    earlier = order[None, :] < order[:, None]
    same_owner = owners[..., :, None] == owners[..., None, :]
    return jnp.sum(jnp.logical_and(same_owner, earlier), axis=-1)


def on_device(queries, key_cache, value_cache, lengths, row_adapter_index, down_weight, up_weight):
    decode_attention = attend(queries, key_cache, value_cache, lengths)
    n_req = lax.axis_size("req")
    my_index = lax.axis_index("req")
    slot_total = n_req * CAP
    block_list = row_adapter_index.reshape(n_req, ROWS_PER_INDEX)
    owners = lax.shift_right_logical(block_list, 5)
    ranks = slot_ranks(owners)

    recv_slot = jnp.where(owners == my_index, jnp.arange(n_req)[:, None] * CAP + ranks, -1).reshape(
        n_req * ROWS_PER_INDEX
    )
    recv_onehot = (jnp.arange(slot_total)[:, None] == recv_slot[None, :]).astype(jnp.bfloat16)
    local_adapter = lax.bitwise_and(row_adapter_index, ADP_REQ - 1)
    adapter_onehot = (local_adapter[:, None] == jnp.arange(ADP_REQ)[None, :]).astype(jnp.bfloat16)
    adapter_of_slot = jnp.dot(recv_onehot, adapter_onehot, preferred_element_type=jnp.float32)

    my_rows = lax.dynamic_slice_in_dim(row_adapter_index, my_index * ROWS_PER_INDEX, ROWS_PER_INDEX)
    my_owners = lax.shift_right_logical(my_rows, 5)
    my_ranks = slot_ranks(my_owners)
    send_slot = my_owners * CAP + my_ranks
    send_onehot = (jnp.arange(slot_total)[:, None] == send_slot[None, :]).astype(jnp.bfloat16)
    packed = jnp.dot(send_onehot, decode_attention, preferred_element_type=jnp.float32).astype(
        jnp.bfloat16
    )
    width = packed.shape[1]
    gathered_rows = lax.all_to_all(
        packed.reshape(n_req, CAP, width), "req", 0, 0, tiled=True
    ).reshape(slot_total, width)
    adapter_delta = apply_adapter(gathered_rows, adapter_of_slot, down_weight, up_weight)
    returned = lax.all_to_all(
        adapter_delta.reshape(n_req, CAP, width), "req", 0, 0, tiled=True
    ).reshape(slot_total, width)
    adapter_output = lax.dot_general(
        send_onehot, returned, (((0,), (0,)), ((), ())), preferred_element_type=jnp.float32
    ).astype(jnp.bfloat16)
    return (decode_attention, adapter_output)


def solution(mesh):
    in_specs = (
        P("req", "tp"),
        P("req", None, "tp"),
        P("req", None, "tp"),
        P("req"),
        P(),
        P("req", "tp", None),
        P("req", None, "tp"),
    )
    out_specs = (P("req", "tp"), P("req", "tp"))
    return jax.shard_map(
        on_device, mesh=mesh, in_specs=in_specs, out_specs=out_specs, check_vma=False
    )
```

```python
import jax
import jax.numpy as jnp
from jax import lax
from jax.sharding import PartitionSpec as P

HEAD_DIM = 128
CAP = 8
ROWS_PER_INDEX = 64
CTX = 64
ADP_REQ = 32
GROUP = 8


def attend(queries, key_cache, value_cache, lengths):
    count = queries.shape[0]
    kv_local = key_cache.shape[2] // HEAD_DIM
    query_heads = queries.reshape(count, kv_local, GROUP, HEAD_DIM)
    key_heads = key_cache.reshape(count, CTX, kv_local, HEAD_DIM)
    value_heads = value_cache.reshape(count, CTX, kv_local, HEAD_DIM)
    scores = jnp.einsum(
        "rkgd,rckd->rkgc", query_heads, key_heads, preferred_element_type=jnp.float32
    ) * HEAD_DIM ** (-0.5)
    valid = jnp.arange(CTX)[None, :] < lengths[:, None]
    scores = jnp.where(valid[:, None, None, :], scores, -jnp.inf)
    highest = jnp.max(scores, axis=3, keepdims=True)
    expo = jnp.exp(scores - highest)
    weights = (expo / jnp.sum(expo, axis=3, keepdims=True)).astype(jnp.bfloat16)
    mixed = jnp.einsum("rkgc,rckd->rkgd", weights, value_heads, preferred_element_type=jnp.float32)
    return mixed.astype(jnp.bfloat16).reshape(count, kv_local * GROUP * HEAD_DIM)


def tree_sum(value, axis):
    size = lax.axis_size(axis)
    step = 1
    while step < size:
        pairs = [(i, i ^ step) for i in range(size)]
        sent = value.astype(jnp.bfloat16)
        value = sent.astype(jnp.float32) + lax.ppermute(sent, axis, pairs).astype(jnp.float32)
        step *= 2
    return value


def apply_adapter(incoming_slots, adapter_of_slot, down_weight, up_weight):
    adapter_grouped = jnp.einsum(
        "pv,hvo->pho", incoming_slots, down_weight, preferred_element_type=jnp.float32
    )
    partial_shrink = jnp.einsum("sar,sa->sr", adapter_grouped, adapter_of_slot)
    shrink = tree_sum(partial_shrink, "tp").astype(jnp.bfloat16)
    spread_rows = shrink[:, None, :] * adapter_of_slot.astype(jnp.bfloat16)[:, :, None]
    return jnp.einsum(
        "fmb,mbc->fc", spread_rows, up_weight, preferred_element_type=jnp.float32
    ).astype(jnp.bfloat16)


def slot_ranks(owners):
    order = jnp.arange(owners.shape[-1])
    earlier = order[None, :] < order[:, None]
    same_owner = owners[..., :, None] == owners[..., None, :]
    return jnp.sum(jnp.logical_and(same_owner, earlier), axis=-1)


def on_device(queries, key_cache, value_cache, lengths, row_adapter_index, down_weight, up_weight):
    decode_attention = attend(queries, key_cache, value_cache, lengths)
    n_req = lax.axis_size("req")
    my_index = lax.axis_index("req")
    slot_total = n_req * CAP
    block_list = row_adapter_index.reshape(n_req, ROWS_PER_INDEX)
    owners = block_list // ADP_REQ
    ranks = slot_ranks(owners)

    recv_slot = jnp.where(owners == my_index, jnp.arange(n_req)[:, None] * CAP + ranks, -1).reshape(
        n_req * ROWS_PER_INDEX
    )
    recv_onehot = (jnp.arange(slot_total)[:, None] == recv_slot[None, :]).astype(jnp.bfloat16)
    local_adapter = row_adapter_index % ADP_REQ
    adapter_onehot = (local_adapter[:, None] == jnp.arange(ADP_REQ)[None, :]).astype(jnp.bfloat16)
    adapter_of_slot = jnp.dot(recv_onehot, adapter_onehot, preferred_element_type=jnp.float32)

    my_owners = lax.dynamic_index_in_dim(owners, my_index, 0, keepdims=False)
    my_ranks = lax.dynamic_index_in_dim(ranks, my_index, 0, keepdims=False)
    send_slot = my_owners * CAP + my_ranks
    send_onehot = (jnp.arange(slot_total)[:, None] == send_slot[None, :]).astype(jnp.bfloat16)
    packed = jnp.dot(send_onehot, decode_attention, preferred_element_type=jnp.float32).astype(
        jnp.bfloat16
    )
    width = packed.shape[1]
    gathered_rows = lax.all_to_all(
        packed.reshape(n_req, CAP, width), "req", 0, 0, tiled=True
    ).reshape(slot_total, width)
    adapter_delta = apply_adapter(gathered_rows, adapter_of_slot, down_weight, up_weight)
    returned = lax.all_to_all(
        adapter_delta.reshape(n_req, CAP, width), "req", 0, 0, tiled=True
    ).reshape(slot_total, width)
    adapter_output = lax.dot_general(
        send_onehot, returned, (((0,), (0,)), ((), ())), preferred_element_type=jnp.float32
    ).astype(jnp.bfloat16)
    return (decode_attention, adapter_output)


def solution(mesh):
    in_specs = (
        P("req", "tp"),
        P("req", None, "tp"),
        P("req", None, "tp"),
        P("req"),
        P(),
        P("req", "tp", None),
        P("req", None, "tp"),
    )
    out_specs = (P("req", "tp"), P("req", "tp"))
    return jax.shard_map(
        on_device, mesh=mesh, in_specs=in_specs, out_specs=out_specs, check_vma=False
    )
```

```python
import jax
import jax.numpy as jnp
from jax import lax
from jax.sharding import PartitionSpec as P

HEAD_DIM = 128
CAP = 8
ROWS_PER_INDEX = 64
CTX = 64
ADP_REQ = 32
GROUP = 8


def attend(queries, key_cache, value_cache, lengths):
    count = queries.shape[0]
    kv_local = key_cache.shape[2] // HEAD_DIM
    query_heads = queries.reshape(count, kv_local, GROUP, HEAD_DIM)
    key_heads = key_cache.reshape(count, CTX, kv_local, HEAD_DIM)
    value_heads = value_cache.reshape(count, CTX, kv_local, HEAD_DIM)
    scores = jnp.einsum(
        "rkgd,rckd->rkgc", query_heads, key_heads, preferred_element_type=jnp.float32
    ) * HEAD_DIM ** (-0.5)
    valid = jnp.arange(CTX)[None, :] < lengths[:, None]
    scores = jnp.where(valid[:, None, None, :], scores, -jnp.inf)
    highest = jnp.max(scores, axis=3, keepdims=True)
    expo = jnp.exp(scores - highest)
    weights = (expo / jnp.sum(expo, axis=3, keepdims=True)).astype(jnp.bfloat16)
    mixed = jnp.einsum("rkgc,rckd->rkgd", weights, value_heads, preferred_element_type=jnp.float32)
    return mixed.astype(jnp.bfloat16).reshape(count, kv_local * GROUP * HEAD_DIM)


def tree_sum(value, axis):
    size = lax.axis_size(axis)
    step = 1
    while step < size:
        pairs = [(i, i ^ step) for i in range(size)]
        value = value + lax.ppermute(value, axis, pairs)
        step *= 2
    return value


def apply_adapter(incoming_slots, adapter_of_slot, down_weight, up_weight):
    adapter_grouped = jnp.einsum(
        "pv,hvo->pho", incoming_slots, down_weight, preferred_element_type=jnp.float32
    )
    partial_shrink = jnp.einsum("sar,sa->sr", adapter_grouped, adapter_of_slot)
    shrink = tree_sum(partial_shrink, "tp").astype(jnp.bfloat16)
    spread_rows = shrink[:, None, :] * adapter_of_slot.astype(jnp.bfloat16)[:, :, None]
    return jnp.einsum(
        "fmb,mbc->fc", spread_rows, up_weight, preferred_element_type=jnp.float32
    ).astype(jnp.bfloat16)


def slot_ranks(owners):
    order = jnp.arange(owners.shape[-1])
    earlier = order[None, :] < order[:, None]
    same_owner = owners[..., :, None] == owners[..., None, :]
    return jnp.sum(jnp.logical_and(same_owner, earlier), axis=-1)


def on_device(queries, key_cache, value_cache, lengths, row_adapter_index, down_weight, up_weight):
    n_req = lax.axis_size("req")
    warm = lax.all_to_all(
        jnp.broadcast_to(queries[:1, :HEAD_DIM], (n_req, CAP, HEAD_DIM)), "req", 0, 0, tiled=True
    )
    decode_attention = attend(queries, key_cache, value_cache, lengths)
    my_index = lax.axis_index("req")
    slot_total = n_req * CAP
    block_list = row_adapter_index.reshape(n_req, ROWS_PER_INDEX)
    owners = block_list // ADP_REQ
    ranks = slot_ranks(owners)

    recv_slot = jnp.where(owners == my_index, jnp.arange(n_req)[:, None] * CAP + ranks, -1).reshape(
        n_req * ROWS_PER_INDEX
    )
    recv_onehot = (jnp.arange(slot_total)[:, None] == recv_slot[None, :]).astype(jnp.bfloat16)
    local_adapter = row_adapter_index % ADP_REQ
    adapter_onehot = (local_adapter[:, None] == jnp.arange(ADP_REQ)[None, :]).astype(jnp.bfloat16)
    adapter_of_slot = jnp.dot(recv_onehot, adapter_onehot, preferred_element_type=jnp.float32)

    my_owners = lax.dynamic_index_in_dim(owners, my_index, 0, keepdims=False)
    my_ranks = lax.dynamic_index_in_dim(ranks, my_index, 0, keepdims=False)
    send_slot = my_owners * CAP + my_ranks
    send_onehot = (jnp.arange(slot_total)[:, None] == send_slot[None, :]).astype(jnp.bfloat16)
    packed = jnp.dot(send_onehot, decode_attention, preferred_element_type=jnp.float32).astype(
        jnp.bfloat16
    )
    never = warm[0, 0, 0] != warm[0, 0, 0]
    packed = jnp.where(never, jnp.zeros_like(packed), packed)
    width = packed.shape[1]
    gathered_rows = lax.all_to_all(
        packed.reshape(n_req, CAP, width), "req", 0, 0, tiled=True
    ).reshape(slot_total, width)
    adapter_delta = apply_adapter(gathered_rows, adapter_of_slot, down_weight, up_weight)
    returned = lax.all_to_all(
        adapter_delta.reshape(n_req, CAP, width), "req", 0, 0, tiled=True
    ).reshape(slot_total, width)
    adapter_output = lax.dot_general(
        send_onehot, returned, (((0,), (0,)), ((), ())), preferred_element_type=jnp.float32
    ).astype(jnp.bfloat16)
    return (decode_attention, adapter_output)


def solution(mesh):
    in_specs = (
        P("req", "tp"),
        P("req", None, "tp"),
        P("req", None, "tp"),
        P("req"),
        P(),
        P("req", "tp", None),
        P("req", None, "tp"),
    )
    out_specs = (P("req", "tp"), P("req", "tp"))
    return jax.shard_map(
        on_device, mesh=mesh, in_specs=in_specs, out_specs=out_specs, check_vma=False
    )
```

```python
import jax
import jax.numpy as jnp
from jax import lax
from jax.experimental import pallas as pl
from jax.experimental.pallas import tpu as pltpu
from jax.sharding import PartitionSpec as P

HEAD_DIM = 128
CAP = 8
ROWS_PER_INDEX = 64
CTX = 64
ADP_REQ = 32
GROUP = 8


def attend(queries, key_cache, value_cache, lengths):
    count = queries.shape[0]
    kv_local = key_cache.shape[2] // HEAD_DIM
    query_heads = queries.reshape(count, kv_local, GROUP, HEAD_DIM)
    key_heads = key_cache.reshape(count, CTX, kv_local, HEAD_DIM)
    value_heads = value_cache.reshape(count, CTX, kv_local, HEAD_DIM)
    scores = jnp.einsum(
        "rkgd,rckd->rkgc", query_heads, key_heads, preferred_element_type=jnp.float32
    ) * HEAD_DIM ** (-0.5)
    valid = jnp.arange(CTX)[None, :] < lengths[:, None]
    scores = jnp.where(valid[:, None, None, :], scores, -jnp.inf)
    highest = jnp.max(scores, axis=3, keepdims=True)
    expo = jnp.exp(scores - highest)
    weights = (expo / jnp.sum(expo, axis=3, keepdims=True)).astype(jnp.bfloat16)
    mixed = jnp.einsum("rkgc,rckd->rkgd", weights, value_heads, preferred_element_type=jnp.float32)
    return mixed.astype(jnp.bfloat16).reshape(count, kv_local * GROUP * HEAD_DIM)


def tree_sum(value, axis):
    size = lax.axis_size(axis)
    step = 1
    while step < size:
        pairs = [(i, i ^ step) for i in range(size)]
        value = value + lax.ppermute(value, axis, pairs)
        step *= 2
    return value


def _to_vmem_body(src_ref, dst_ref, sem):
    copy = pltpu.make_async_copy(src_ref, dst_ref, sem)
    copy.start()
    copy.wait()


def to_vmem(array):
    size = array.size * array.dtype.itemsize
    return pl.pallas_call(
        _to_vmem_body,
        out_shape=jax.ShapeDtypeStruct(array.shape, array.dtype),
        in_specs=[pl.BlockSpec(memory_space=pl.ANY)],
        out_specs=pl.BlockSpec(memory_space=pltpu.VMEM),
        scratch_shapes=[pltpu.SemaphoreType.DMA(())],
        compiler_params=pltpu.CompilerParams(vmem_limit_bytes=32 * 1024 * 1024),
        cost_estimate=pl.CostEstimate(flops=0, transcendentals=0, bytes_accessed=2 * size),
    )(array)


def apply_adapter(incoming_slots, adapter_of_slot, down_weight, up_weight):
    down_on_chip = to_vmem(jnp.swapaxes(down_weight, 1, 2))
    adapter_grouped = jnp.einsum(
        "pv,hov->pho", incoming_slots, down_on_chip, preferred_element_type=jnp.float32
    )
    partial_shrink = jnp.einsum("sar,sa->sr", adapter_grouped, adapter_of_slot)
    shrink = tree_sum(partial_shrink, "tp").astype(jnp.bfloat16)
    spread_rows = shrink[:, None, :] * adapter_of_slot.astype(jnp.bfloat16)[:, :, None]
    return jnp.einsum(
        "fmb,mbc->fc", spread_rows, up_weight, preferred_element_type=jnp.float32
    ).astype(jnp.bfloat16)


def slot_ranks(owners):
    order = jnp.arange(owners.shape[-1])
    earlier = order[None, :] < order[:, None]
    same_owner = owners[..., :, None] == owners[..., None, :]
    return jnp.sum(jnp.logical_and(same_owner, earlier), axis=-1)


def on_device(queries, key_cache, value_cache, lengths, row_adapter_index, down_weight, up_weight):
    decode_attention = attend(queries, key_cache, value_cache, lengths)
    n_req = lax.axis_size("req")
    my_index = lax.axis_index("req")
    slot_total = n_req * CAP
    block_list = row_adapter_index.reshape(n_req, ROWS_PER_INDEX)
    owners = block_list // ADP_REQ
    ranks = slot_ranks(owners)

    recv_slot = jnp.where(owners == my_index, jnp.arange(n_req)[:, None] * CAP + ranks, -1).reshape(
        n_req * ROWS_PER_INDEX
    )
    recv_onehot = (jnp.arange(slot_total)[:, None] == recv_slot[None, :]).astype(jnp.bfloat16)
    local_adapter = row_adapter_index % ADP_REQ
    adapter_onehot = (local_adapter[:, None] == jnp.arange(ADP_REQ)[None, :]).astype(jnp.bfloat16)
    adapter_of_slot = jnp.dot(recv_onehot, adapter_onehot, preferred_element_type=jnp.float32)

    my_owners = lax.dynamic_index_in_dim(owners, my_index, 0, keepdims=False)
    my_ranks = lax.dynamic_index_in_dim(ranks, my_index, 0, keepdims=False)
    send_slot = my_owners * CAP + my_ranks
    send_onehot = (jnp.arange(slot_total)[:, None] == send_slot[None, :]).astype(jnp.bfloat16)
    packed = jnp.dot(send_onehot, decode_attention, preferred_element_type=jnp.float32).astype(
        jnp.bfloat16
    )
    width = packed.shape[1]
    gathered_rows = lax.all_to_all(
        packed.reshape(n_req, CAP, width), "req", 0, 0, tiled=True
    ).reshape(slot_total, width)
    adapter_delta = apply_adapter(gathered_rows, adapter_of_slot, down_weight, up_weight)
    returned = lax.all_to_all(
        adapter_delta.reshape(n_req, CAP, width), "req", 0, 0, tiled=True
    ).reshape(slot_total, width)
    adapter_output = lax.dot_general(
        send_onehot, returned, (((0,), (0,)), ((), ())), preferred_element_type=jnp.float32
    ).astype(jnp.bfloat16)
    return (decode_attention, adapter_output)


def solution(mesh):
    in_specs = (
        P("req", "tp"),
        P("req", None, "tp"),
        P("req", None, "tp"),
        P("req"),
        P(),
        P("req", "tp", None),
        P("req", None, "tp"),
    )
    out_specs = (P("req", "tp"), P("req", "tp"))
    return jax.shard_map(
        on_device, mesh=mesh, in_specs=in_specs, out_specs=out_specs, check_vma=False
    )
```

```python
import jax
import jax.numpy as jnp
from jax import lax
from jax.sharding import PartitionSpec as P


HEAD_DIM = 128
CAP = 8
ROWS_PER_INDEX = 64
CTX = 64
ADP_REQ = 32
GROUP = 8


def attend(queries, key_cache, value_cache, lengths):
    count = queries.shape[0]
    kv_local = key_cache.shape[2] // HEAD_DIM
    query_heads = queries.reshape(count, kv_local, GROUP, HEAD_DIM)
    key_heads = key_cache.reshape(count, CTX, kv_local, HEAD_DIM)
    value_heads = value_cache.reshape(count, CTX, kv_local, HEAD_DIM)
    scores = jnp.einsum(
        "rkgd,rckd->rkgc", query_heads, key_heads, preferred_element_type=jnp.float32
    ) * HEAD_DIM ** (-0.5)
    valid = jnp.arange(CTX)[None, :] < lengths[:, None]
    scores = jnp.where(valid[:, None, None, :], scores, -jnp.inf)
    highest = jnp.max(scores, axis=3, keepdims=True)
    expo = jnp.exp(scores - highest)
    weights = (expo / jnp.sum(expo, axis=3, keepdims=True)).astype(jnp.bfloat16)
    mixed = jnp.einsum("rkgc,rckd->rkgd", weights, value_heads, preferred_element_type=jnp.float32)
    return mixed.astype(jnp.bfloat16).reshape(count, kv_local * GROUP * HEAD_DIM)


def pair_ring_sum(value, axis):
    size = lax.axis_size(axis)
    value = value + lax.ppermute(value, axis, [(i, i ^ 1) for i in range(size)])
    chips = size // 2
    me = lax.axis_index(axis) // 2
    parts = [value] + [
        lax.ppermute(value, axis, [(i, (i + 2 * k) % size) for i in range(size)])
        for k in range(1, chips)
    ]
    stacked = jnp.flip(jnp.stack(parts, axis=0), axis=0)
    stacked = jnp.roll(stacked, me + 1, axis=0)
    return jnp.sum(stacked, axis=0)


def apply_adapter(incoming_slots, adapter_of_slot, down_weight, up_weight):
    adapter_grouped = jnp.einsum(
        "pv,hvo->pho", incoming_slots, down_weight, preferred_element_type=jnp.float32
    )
    partial_shrink = jnp.einsum("sar,sa->sr", adapter_grouped, adapter_of_slot)
    shrink = pair_ring_sum(partial_shrink, "tp").astype(jnp.bfloat16)
    spread_rows = shrink[:, None, :] * adapter_of_slot.astype(jnp.bfloat16)[:, :, None]
    return jnp.einsum(
        "fmb,mbc->fc", spread_rows, up_weight, preferred_element_type=jnp.float32
    ).astype(jnp.bfloat16)


def slot_ranks(owners):
    order = jnp.arange(owners.shape[-1])
    earlier = order[None, :] < order[:, None]
    same_owner = owners[..., :, None] == owners[..., None, :]
    return jnp.sum(jnp.logical_and(same_owner, earlier), axis=-1)


def on_device(queries, key_cache, value_cache, lengths, row_adapter_index, down_weight, up_weight):
    decode_attention = attend(queries, key_cache, value_cache, lengths)
    n_req = lax.axis_size("req")
    my_index = lax.axis_index("req")
    slot_total = n_req * CAP
    block_list = row_adapter_index.reshape(n_req, ROWS_PER_INDEX)
    owners = block_list // ADP_REQ
    ranks = slot_ranks(owners)

    recv_slot = jnp.where(owners == my_index, jnp.arange(n_req)[:, None] * CAP + ranks, -1).reshape(
        n_req * ROWS_PER_INDEX
    )
    recv_onehot = (jnp.arange(slot_total)[:, None] == recv_slot[None, :]).astype(jnp.bfloat16)
    local_adapter = row_adapter_index % ADP_REQ
    adapter_onehot = (local_adapter[:, None] == jnp.arange(ADP_REQ)[None, :]).astype(jnp.bfloat16)
    adapter_of_slot = jnp.dot(recv_onehot, adapter_onehot, preferred_element_type=jnp.float32)

    my_owners = lax.dynamic_index_in_dim(owners, my_index, 0, keepdims=False)
    my_ranks = lax.dynamic_index_in_dim(ranks, my_index, 0, keepdims=False)
    send_slot = my_owners * CAP + my_ranks
    send_onehot = (jnp.arange(slot_total)[:, None] == send_slot[None, :]).astype(jnp.bfloat16)
    packed = jnp.dot(send_onehot, decode_attention, preferred_element_type=jnp.float32).astype(
        jnp.bfloat16
    )
    width = packed.shape[1]
    gathered_rows = lax.all_to_all(
        packed.reshape(n_req, CAP, width), "req", 0, 0, tiled=True
    ).reshape(slot_total, width)
    adapter_delta = apply_adapter(gathered_rows, adapter_of_slot, down_weight, up_weight)
    returned = lax.all_to_all(
        adapter_delta.reshape(n_req, CAP, width), "req", 0, 0, tiled=True
    ).reshape(slot_total, width)
    adapter_output = lax.dot_general(
        send_onehot, returned, (((0,), (0,)), ((), ())), preferred_element_type=jnp.float32
    ).astype(jnp.bfloat16)
    return (decode_attention, adapter_output)


def solution(mesh):
    in_specs = (
        P("req", "tp"),
        P("req", None, "tp"),
        P("req", None, "tp"),
        P("req"),
        P(),
        P("req", "tp", None),
        P("req", None, "tp"),
    )
    out_specs = (P("req", "tp"), P("req", "tp"))
    return jax.shard_map(
        on_device, mesh=mesh, in_specs=in_specs, out_specs=out_specs, check_vma=False
    )
```

```python
import jax
import jax.numpy as jnp
from jax import lax
from jax.experimental import pallas as pl
from jax.experimental.pallas import tpu as pltpu
from jax.sharding import PartitionSpec as P


HEAD_DIM = 128
CAP = 8
ROWS_PER_INDEX = 64
CTX = 64
ADP_REQ = 32
GROUP = 8


def attend(queries, key_cache, value_cache, lengths):
    count = queries.shape[0]
    kv_local = key_cache.shape[2] // HEAD_DIM
    query_heads = queries.reshape(count, kv_local, GROUP, HEAD_DIM)
    key_heads = key_cache.reshape(count, CTX, kv_local, HEAD_DIM)
    value_heads = value_cache.reshape(count, CTX, kv_local, HEAD_DIM)
    scores = jnp.einsum(
        "rkgd,rckd->rkgc", query_heads, key_heads, preferred_element_type=jnp.float32
    ) * HEAD_DIM ** (-0.5)
    valid = jnp.arange(CTX)[None, :] < lengths[:, None]
    scores = jnp.where(valid[:, None, None, :], scores, -jnp.inf)
    highest = jnp.max(scores, axis=3, keepdims=True)
    expo = jnp.exp(scores - highest)
    weights = (expo / jnp.sum(expo, axis=3, keepdims=True)).astype(jnp.bfloat16)
    mixed = jnp.einsum("rkgc,rckd->rkgd", weights, value_heads, preferred_element_type=jnp.float32)
    return mixed.astype(jnp.bfloat16).reshape(count, kv_local * GROUP * HEAD_DIM)


def pair_ring_sum(value, axis):
    size = lax.axis_size(axis)
    value = value + lax.ppermute(value, axis, [(i, i ^ 1) for i in range(size)])
    chips = size // 2
    me = lax.axis_index(axis) // 2
    parts = [value] + [
        lax.ppermute(value, axis, [(i, (i + 2 * k) % size) for i in range(size)])
        for k in range(1, chips)
    ]
    stacked = jnp.flip(jnp.stack(parts, axis=0), axis=0)
    stacked = jnp.roll(stacked, me + 1, axis=0)
    return jnp.sum(stacked, axis=0)


def _up_body(s_ref, sel_ref, u_ref, o_ref):
    rank = s_ref.shape[1]
    adapters = sel_ref.shape[1]
    shift = rank.bit_length() - 1
    col = lax.broadcasted_iota(jnp.int32, (rank, adapters * rank), 1)
    row = lax.broadcasted_iota(jnp.int32, (rank, adapters * rank), 0)
    repeat = (lax.bitwise_and(col, rank - 1) == row).astype(jnp.bfloat16)
    col = lax.broadcasted_iota(jnp.int32, (adapters, adapters * rank), 1)
    row = lax.broadcasted_iota(jnp.int32, (adapters, adapters * rank), 0)
    expand = (lax.shift_right_logical(col, shift) == row).astype(jnp.bfloat16)
    spread = jnp.dot(s_ref[...], repeat, preferred_element_type=jnp.float32) * jnp.dot(
        sel_ref[...], expand, preferred_element_type=jnp.float32
    )
    o_ref[...] = jnp.dot(
        spread.astype(jnp.bfloat16), u_ref[...], preferred_element_type=jnp.float32
    ).astype(o_ref.dtype)


def up_project(shrink, adapter_of_slot, up_weight):
    adapters, rank, width = up_weight.shape
    slots = shrink.shape[0]
    return pl.pallas_call(
        _up_body,
        out_shape=jax.ShapeDtypeStruct((slots, width), jnp.bfloat16),
        in_specs=[pl.BlockSpec(memory_space=pltpu.VMEM)] * 3,
        out_specs=pl.BlockSpec(memory_space=pltpu.VMEM),
        compiler_params=pltpu.CompilerParams(vmem_limit_bytes=32 * 1024 * 1024),
        cost_estimate=pl.CostEstimate(
            flops=2 * slots * adapters * rank * (width + rank + adapters),
            transcendentals=0,
            bytes_accessed=2 * (adapters * rank * width + slots * (width + rank + adapters)),
        ),
    )(shrink, adapter_of_slot, up_weight.reshape(adapters * rank, width))


def apply_adapter(incoming_slots, adapter_of_slot, down_weight, up_weight):
    adapter_grouped = jnp.einsum(
        "pv,hvo->pho", incoming_slots, down_weight, preferred_element_type=jnp.float32
    )
    partial_shrink = jnp.einsum("sar,sa->sr", adapter_grouped, adapter_of_slot)
    shrink = pair_ring_sum(partial_shrink, "tp").astype(jnp.bfloat16)
    return up_project(shrink, adapter_of_slot.astype(jnp.bfloat16), up_weight)


def slot_ranks(owners):
    order = jnp.arange(owners.shape[-1])
    earlier = order[None, :] < order[:, None]
    same_owner = owners[..., :, None] == owners[..., None, :]
    return jnp.sum(jnp.logical_and(same_owner, earlier), axis=-1)


def on_device(queries, key_cache, value_cache, lengths, row_adapter_index, down_weight, up_weight):
    decode_attention = attend(queries, key_cache, value_cache, lengths)
    n_req = lax.axis_size("req")
    my_index = lax.axis_index("req")
    slot_total = n_req * CAP
    block_list = row_adapter_index.reshape(n_req, ROWS_PER_INDEX)
    owners = block_list // ADP_REQ
    ranks = slot_ranks(owners)

    recv_slot = jnp.where(owners == my_index, jnp.arange(n_req)[:, None] * CAP + ranks, -1).reshape(
        n_req * ROWS_PER_INDEX
    )
    recv_onehot = (jnp.arange(slot_total)[:, None] == recv_slot[None, :]).astype(jnp.bfloat16)
    local_adapter = row_adapter_index % ADP_REQ
    adapter_onehot = (local_adapter[:, None] == jnp.arange(ADP_REQ)[None, :]).astype(jnp.bfloat16)
    adapter_of_slot = jnp.dot(recv_onehot, adapter_onehot, preferred_element_type=jnp.float32)

    my_owners = lax.dynamic_index_in_dim(owners, my_index, 0, keepdims=False)
    my_ranks = lax.dynamic_index_in_dim(ranks, my_index, 0, keepdims=False)
    send_slot = my_owners * CAP + my_ranks
    send_onehot = (jnp.arange(slot_total)[:, None] == send_slot[None, :]).astype(jnp.bfloat16)
    packed = jnp.dot(send_onehot, decode_attention, preferred_element_type=jnp.float32).astype(
        jnp.bfloat16
    )
    width = packed.shape[1]
    gathered_rows = lax.all_to_all(
        packed.reshape(n_req, CAP, width), "req", 0, 0, tiled=True
    ).reshape(slot_total, width)
    adapter_delta = apply_adapter(gathered_rows, adapter_of_slot, down_weight, up_weight)
    returned = lax.all_to_all(
        adapter_delta.reshape(n_req, CAP, width), "req", 0, 0, tiled=True
    ).reshape(slot_total, width)
    adapter_output = lax.dot_general(
        send_onehot, returned, (((0,), (0,)), ((), ())), preferred_element_type=jnp.float32
    ).astype(jnp.bfloat16)
    return (decode_attention, adapter_output)


def solution(mesh):
    in_specs = (
        P("req", "tp"),
        P("req", None, "tp"),
        P("req", None, "tp"),
        P("req"),
        P(),
        P("req", "tp", None),
        P("req", None, "tp"),
    )
    out_specs = (P("req", "tp"), P("req", "tp"))
    return jax.shard_map(
        on_device, mesh=mesh, in_specs=in_specs, out_specs=out_specs, check_vma=False
    )
```

```python
import jax
import jax.numpy as jnp
from jax import lax
from jax.experimental import pallas as pl
from jax.experimental.pallas import tpu as pltpu
from jax.sharding import PartitionSpec as P

HEAD_DIM = 128
CAP = 8
ROWS_PER_INDEX = 64
CTX = 64
ADP_REQ = 32
GROUP = 8


def attend(queries, key_cache, value_cache, lengths):
    count = queries.shape[0]
    kv_local = key_cache.shape[2] // HEAD_DIM
    query_heads = queries.reshape(count, kv_local, GROUP, HEAD_DIM)
    key_heads = key_cache.reshape(count, CTX, kv_local, HEAD_DIM)
    value_heads = value_cache.reshape(count, CTX, kv_local, HEAD_DIM)
    scores = jnp.einsum(
        "rkgd,rckd->rkgc", query_heads, key_heads, preferred_element_type=jnp.float32
    ) * HEAD_DIM ** (-0.5)
    valid = jnp.arange(CTX)[None, :] < lengths[:, None]
    scores = jnp.where(valid[:, None, None, :], scores, -jnp.inf)
    highest = jnp.max(scores, axis=3, keepdims=True)
    expo = jnp.exp(scores - highest)
    weights = (expo / jnp.sum(expo, axis=3, keepdims=True)).astype(jnp.bfloat16)
    mixed = jnp.einsum("rkgc,rckd->rkgd", weights, value_heads, preferred_element_type=jnp.float32)
    return mixed.astype(jnp.bfloat16).reshape(count, kv_local * GROUP * HEAD_DIM)


def tree_sum(value, axis):
    size = lax.axis_size(axis)
    step = 1
    while step < size:
        pairs = [(i, i ^ step) for i in range(size)]
        value = value + lax.ppermute(value, axis, pairs)
        step *= 2
    return value


def _to_vmem_body(src_ref, dst_ref, sem):
    copy = pltpu.make_async_copy(src_ref, dst_ref, sem)
    copy.start()
    copy.wait()


def to_vmem(array):
    size = array.size * array.dtype.itemsize
    return pl.pallas_call(
        _to_vmem_body,
        out_shape=jax.ShapeDtypeStruct(array.shape, array.dtype),
        in_specs=[pl.BlockSpec(memory_space=pl.ANY)],
        out_specs=pl.BlockSpec(memory_space=pltpu.VMEM),
        scratch_shapes=[pltpu.SemaphoreType.DMA(())],
        compiler_params=pltpu.CompilerParams(vmem_limit_bytes=32 * 1024 * 1024),
        cost_estimate=pl.CostEstimate(flops=0, transcendentals=0, bytes_accessed=2 * size),
    )(array)


def apply_adapter(incoming_slots, adapter_of_slot, down_weight, up_weight):
    down_on_chip = to_vmem(jnp.swapaxes(down_weight, 1, 2))
    adapter_grouped = jnp.einsum(
        "pv,hov->pho", incoming_slots, down_on_chip, preferred_element_type=jnp.float32
    )
    partial_shrink = jnp.einsum("sar,sa->sr", adapter_grouped, adapter_of_slot)
    shrink = tree_sum(partial_shrink, "tp").astype(jnp.bfloat16)
    spread_rows = shrink[:, None, :] * adapter_of_slot.astype(jnp.bfloat16)[:, :, None]
    return jnp.einsum(
        "fmb,mbc->fc", spread_rows, up_weight, preferred_element_type=jnp.float32
    ).astype(jnp.bfloat16)


def slot_ranks(owners):
    order = jnp.arange(owners.shape[-1])
    earlier = order[None, :] < order[:, None]
    same_owner = owners[..., :, None] == owners[..., None, :]
    return jnp.sum(jnp.logical_and(same_owner, earlier), axis=-1)


def on_device(queries, key_cache, value_cache, lengths, row_adapter_index, down_weight, up_weight):
    decode_attention = attend(queries, key_cache, value_cache, lengths)
    n_req = lax.axis_size("req")
    my_index = lax.axis_index("req")
    slot_total = n_req * CAP
    block_list = row_adapter_index.reshape(n_req, ROWS_PER_INDEX)
    owners = block_list // ADP_REQ
    ranks = slot_ranks(owners)

    recv_slot = jnp.where(owners == my_index, jnp.arange(n_req)[:, None] * CAP + ranks, -1).reshape(
        n_req * ROWS_PER_INDEX
    )
    recv_onehot = (jnp.arange(slot_total)[:, None] == recv_slot[None, :]).astype(jnp.bfloat16)
    local_adapter = row_adapter_index % ADP_REQ
    adapter_onehot = (local_adapter[:, None] == jnp.arange(ADP_REQ)[None, :]).astype(jnp.bfloat16)
    adapter_of_slot = jnp.dot(recv_onehot, adapter_onehot, preferred_element_type=jnp.float32)

    my_rows = lax.dynamic_slice_in_dim(row_adapter_index, my_index * ROWS_PER_INDEX, ROWS_PER_INDEX)
    my_owners = my_rows // ADP_REQ
    my_ranks = slot_ranks(my_owners)
    send_slot = my_owners * CAP + my_ranks
    send_onehot = (jnp.arange(slot_total)[:, None] == send_slot[None, :]).astype(jnp.bfloat16)
    packed = jnp.dot(send_onehot, decode_attention, preferred_element_type=jnp.float32).astype(
        jnp.bfloat16
    )
    width = packed.shape[1]
    gathered_rows = lax.all_to_all(
        packed.reshape(n_req, CAP, width), "req", 0, 0, tiled=True
    ).reshape(slot_total, width)
    adapter_delta = apply_adapter(gathered_rows, adapter_of_slot, down_weight, up_weight)
    returned = lax.all_to_all(
        adapter_delta.reshape(n_req, CAP, width), "req", 0, 0, tiled=True
    ).reshape(slot_total, width)
    adapter_output = lax.dot_general(
        send_onehot, returned, (((0,), (0,)), ((), ())), preferred_element_type=jnp.float32
    ).astype(jnp.bfloat16)
    return (decode_attention, adapter_output)


def solution(mesh):
    in_specs = (
        P("req", "tp"),
        P("req", None, "tp"),
        P("req", None, "tp"),
        P("req"),
        P(),
        P("req", "tp", None),
        P("req", None, "tp"),
    )
    out_specs = (P("req", "tp"), P("req", "tp"))
    return jax.shard_map(
        on_device, mesh=mesh, in_specs=in_specs, out_specs=out_specs, check_vma=False
    )
```

```python
import jax
import jax.numpy as jnp
from jax import lax
from jax.experimental import pallas as pl
from jax.experimental.pallas import tpu as pltpu
from jax.sharding import PartitionSpec as P

HEAD_DIM = 128
CAP = 8
ROWS_PER_INDEX = 64
CTX = 64
ADP_REQ = 32
GROUP = 8


def attend(queries, key_cache, value_cache, lengths):
    count = queries.shape[0]
    kv_local = key_cache.shape[2] // HEAD_DIM
    query_heads = queries.reshape(count, kv_local, GROUP, HEAD_DIM)
    key_heads = key_cache.reshape(count, CTX, kv_local, HEAD_DIM)
    value_heads = value_cache.reshape(count, CTX, kv_local, HEAD_DIM)
    scores = jnp.einsum(
        "rkgd,rckd->rkgc", query_heads, key_heads, preferred_element_type=jnp.float32
    ) * HEAD_DIM ** (-0.5)
    valid = jnp.arange(CTX)[None, :] < lengths[:, None]
    scores = jnp.where(valid[:, None, None, :], scores, -jnp.inf)
    highest = jnp.max(scores, axis=3, keepdims=True)
    expo = jnp.exp(scores - highest)
    weights = (expo / jnp.sum(expo, axis=3, keepdims=True)).astype(jnp.bfloat16)
    mixed = jnp.einsum("rkgc,rckd->rkgd", weights, value_heads, preferred_element_type=jnp.float32)
    return mixed.astype(jnp.bfloat16).reshape(count, kv_local * GROUP * HEAD_DIM)


def tree_sum(value, axis):
    size = lax.axis_size(axis)
    step = 1
    while step < size:
        pairs = [(i, i ^ step) for i in range(size)]
        value = value + lax.ppermute(value, axis, pairs)
        step *= 2
    return value


def _to_vmem_body(src_ref, dst_ref, sem):
    copy = pltpu.make_async_copy(src_ref, dst_ref, sem)
    copy.start()
    copy.wait()


def to_vmem(array):
    size = array.size * array.dtype.itemsize
    return pl.pallas_call(
        _to_vmem_body,
        out_shape=jax.ShapeDtypeStruct(array.shape, array.dtype),
        in_specs=[pl.BlockSpec(memory_space=pl.ANY)],
        out_specs=pl.BlockSpec(memory_space=pltpu.VMEM),
        scratch_shapes=[pltpu.SemaphoreType.DMA(())],
        compiler_params=pltpu.CompilerParams(vmem_limit_bytes=32 * 1024 * 1024),
        cost_estimate=pl.CostEstimate(flops=0, transcendentals=0, bytes_accessed=2 * size),
    )(array)


def apply_adapter(incoming_slots, adapter_of_slot, down_weight, up_weight):
    down_on_chip = to_vmem(jnp.swapaxes(down_weight, 1, 2))
    adapter_grouped = jnp.einsum(
        "pv,hov->pho", incoming_slots, down_on_chip, preferred_element_type=jnp.float32
    )
    partial_shrink = jnp.einsum("sar,sa->sr", adapter_grouped, adapter_of_slot)
    shrink = tree_sum(partial_shrink, "tp").astype(jnp.bfloat16)
    spread_rows = shrink[:, None, :] * adapter_of_slot.astype(jnp.bfloat16)[:, :, None]
    return jnp.einsum(
        "fmb,mbc->fc", spread_rows, up_weight, preferred_element_type=jnp.float32
    ).astype(jnp.bfloat16)


def slot_ranks(owners):
    order = jnp.arange(owners.shape[-1])
    earlier = order[None, :] < order[:, None]
    same_owner = owners[..., :, None] == owners[..., None, :]
    return jnp.sum(jnp.logical_and(same_owner, earlier), axis=-1)


def on_device(queries, key_cache, value_cache, lengths, row_adapter_index, down_weight, up_weight):
    decode_attention = attend(queries, key_cache, value_cache, lengths)
    n_req = lax.axis_size("req")
    my_index = lax.axis_index("req")
    slot_total = n_req * CAP
    block_list = row_adapter_index.reshape(n_req, ROWS_PER_INDEX)
    owners = lax.shift_right_logical(block_list, 5)
    ranks = slot_ranks(owners)

    recv_slot = jnp.where(owners == my_index, jnp.arange(n_req)[:, None] * CAP + ranks, -1).reshape(
        n_req * ROWS_PER_INDEX
    )
    recv_onehot = (jnp.arange(slot_total)[:, None] == recv_slot[None, :]).astype(jnp.bfloat16)
    local_adapter = lax.bitwise_and(row_adapter_index, ADP_REQ - 1)
    adapter_onehot = (local_adapter[:, None] == jnp.arange(ADP_REQ)[None, :]).astype(jnp.bfloat16)
    adapter_of_slot = jnp.dot(recv_onehot, adapter_onehot, preferred_element_type=jnp.float32)

    my_rows = lax.dynamic_slice_in_dim(row_adapter_index, my_index * ROWS_PER_INDEX, ROWS_PER_INDEX)
    my_owners = lax.shift_right_logical(my_rows, 5)
    my_ranks = slot_ranks(my_owners)
    send_slot = my_owners * CAP + my_ranks
    send_onehot = (jnp.arange(slot_total)[:, None] == send_slot[None, :]).astype(jnp.bfloat16)
    packed = jnp.dot(send_onehot, decode_attention, preferred_element_type=jnp.float32).astype(
        jnp.bfloat16
    )
    width = packed.shape[1]
    gathered_rows = lax.all_to_all(
        packed.reshape(n_req, CAP, width), "req", 0, 0, tiled=True
    ).reshape(slot_total, width)
    adapter_delta = apply_adapter(gathered_rows, adapter_of_slot, down_weight, up_weight)
    returned = lax.all_to_all(
        adapter_delta.reshape(n_req, CAP, width), "req", 0, 0, tiled=True
    ).reshape(slot_total, width)
    adapter_output = lax.dot_general(
        send_onehot, returned, (((0,), (0,)), ((), ())), preferred_element_type=jnp.float32
    ).astype(jnp.bfloat16)
    return (decode_attention, adapter_output)


def solution(mesh):
    in_specs = (
        P("req", "tp"),
        P("req", None, "tp"),
        P("req", None, "tp"),
        P("req"),
        P(),
        P("req", "tp", None),
        P("req", None, "tp"),
    )
    out_specs = (P("req", "tp"), P("req", "tp"))
    return jax.shard_map(
        on_device, mesh=mesh, in_specs=in_specs, out_specs=out_specs, check_vma=False
    )
```
